256 devices in a mesh: expert: 128 (over x, z, y), hid: 2 (over core).
Axes of the slice: x: 4, y: 4, z: 8, core: 2. Of those that a mesh axis runs over, the one named last changes fastest.
Arguments:
- tokens: bfloat16 [16384, 3584], P('expert'), may hold values from -6 to 6
- out_grad: bfloat16 [16384, 3584], P('expert'), may hold values from -4 to 4
- route_ids: int32 [16384, 4], P('expert'), may hold values from 0 to 127, all different within a row; in each aligned block of 128 rows (0 to 127, 128 to 255, ...) at most 6 rows name the same one
- route_gates: float32 [16384, 4], P('expert'), may hold values from 0.1 to 1
- w_gate: bfloat16 [128, 3584, 1024], P('expert', None, 'hid'), may hold values from -0.09375 to 0.09375
- w_up: bfloat16 [128, 3584, 1024], P('expert', None, 'hid'), may hold values from -0.09375 to 0.09375
- w_down: bfloat16 [128, 1024, 3584], P('expert', 'hid'), may hold values from -0.1875 to 0.1875
Outputs:
- token_grad: bfloat16 [16384, 3584], P('expert', 'hid')
- gate_grad: bfloat16 [16384, 4], P('expert')
The draws below stay inside these ranges and needn't reach their ends.
Inputs may be any that keep to these rules, and one draw needn't show every extreme that they name: `route_ids`: each token names 4 different experts. Among the 128 tokens of one index of expert (aligned blocks of rows), no expert is named more than 6 times, a bound that some block reaches.
All inputs are finite; a program needn't handle non-finite values.
Results may differ from the reference program's by a relative error of at most 0.008.
Values may be sent and summed in bfloat16 or wider, within the bound.
No kernel may reach another device: no remote copies, remote signals or barrier semaphores. Data moves between devices by JAX's collectives and lax.ppermute only.
A program may use at most 128 MiB of HBM per device.

```python
import math
import jax
import jax.numpy as jnp
import numpy as np
from jax import lax

D = 3584
FF = 1024
TOP_WIN = 4
TOK_DEV = 128
EXPERTS = 128
CAP = 6
TOKENS = 16384
N_EXPERT = 128


def level_of(own_key, extent, split, smallest, high):
    def one(dim, blocks):
        steps = jax.random.uniform(jax.random.fold_in(jax.random.fold_in(own_key, 6), dim), (blocks,), jnp.float32, smallest / len(split), high / len(split))
        return jnp.repeat(jnp.exp(steps), extent[dim] // blocks).reshape((-1,) + (1,) * (len(extent) - dim - 1))

    gain = one(*split[0])
    for cut in split[1:]:
        gain = gain * one(*cut)
    return gain


def assign_block(key, own, number, rows, count, top, most, slope):
    order = jax.random.permutation(key, count)
    heavy_load, common = portions_of(count, rows * top, most, slope, True), portions_of(count, rows * top, most, slope, False)
    places = jnp.arange(count)

    def named(lengths, turn):
        used = int((lengths > 0).sum())
        fixed = max(1, used // 4)
        shifted = fixed + (places - fixed + turn * (used - fixed)) % max(1, count - fixed)
        return jnp.zeros((count,), jnp.int32).at[order[jnp.where(places < fixed, places, shifted)]].set(jnp.asarray(lengths, jnp.int32))

    lengths = jnp.where(number % 4 == 0, named(heavy_load, number // 4), named(common, number - number // 4 - 1))
    mixed = jax.random.permutation(jax.random.fold_in(own, 3), count)
    giver, sink = mixed[0:count // 2 * 2:2], mixed[1:count // 2 * 2:2]
    slack = jnp.minimum(lengths[giver] - 1, most - lengths[sink]) // 2
    slack = jnp.where((giver == order[0]) | (sink == order[0]) | (lengths[sink] == 0), 0, jnp.maximum(slack, 0))
    shifted = jax.random.randint(jax.random.fold_in(own, 4), (count // 2,), 0, 1 << 20) % (slack + 1)
    lengths = lengths.at[giver].add(-shifted).at[sink].add(shifted)
    items = jnp.searchsorted(jnp.cumsum(lengths), jnp.arange(rows * top), side="right").astype(jnp.int32)
    listing = items.reshape(top, rows).T
    listing = listing[jax.random.permutation(jax.random.fold_in(own, 1), rows)]
    turn = jax.random.randint(jax.random.fold_in(own, 2), (rows, 1), 0, top)
    return jnp.take_along_axis(listing, (jnp.arange(top)[None, :] + turn) % top, axis=1)


def portions_of(count, total, reach, slope, full):
    weights = [(1 << 20) // math.isqrt(rank ** slope) + 1 for rank in range(1, count + 1)]
    largest = reach if full else min(reach, max(-(-total // count), total * weights[0] // sum(weights)))
    least = 1 if total - largest >= count - 1 else 0
    given, surplus = [largest] + [least] * (count - 1), total - largest - least * (count - 1)
    while surplus > 0:
        candidates = [i for i in range(1, count) if given[i] < largest] or [i for i in range(1, count) if given[i] < reach]
        pool, budget = sum([weights[i] for i in candidates]), surplus
        for i in candidates:
            more = min(reach - given[i], max(1, budget * weights[i] // pool), surplus)
            given[i] = given[i] + more
            surplus = surplus - more
    return np.array(given)


def centred(rng, dims, spread, most, cuts=(), kind=jnp.bfloat16):
    entries = spread * jax.random.normal(rng, dims, jnp.float32)
    if cuts:
        entries = entries * level_of(rng, dims, cuts, -0.22, 0.18)
    return jnp.clip(entries, -most, most).astype(kind)


def setup_inputs(seed: int = 0) -> dict:
    key_of = jax.random.split(jax.random.key(seed), 8)
    tokens = centred(key_of[0], (TOKENS, D), 1.0, 6.0, ((0, 128),))
    out_grad = centred(key_of[1], (TOKENS, D), 0.5, 4.0, ((0, 128),))
    route_ids_keys = jax.random.split(jax.random.fold_in(key_of[2], 1), TOKENS // TOK_DEV)
    route_ids_turns = jax.random.permutation(jax.random.fold_in(key_of[2], 3), TOKENS // TOK_DEV)
    route_ids = jax.vmap(lambda own, number: assign_block(jax.random.fold_in(key_of[2], 2), own, number, TOK_DEV, EXPERTS, TOP_WIN, CAP, 1))(route_ids_keys, route_ids_turns).reshape((TOKENS, TOP_WIN))
    route_gates = jnp.clip(0.1 + 0.9 * jax.random.uniform(key_of[3], (TOKENS, TOP_WIN), jnp.float32) ** level_of(key_of[3], (TOKENS, TOP_WIN), ((0, 128),), -0.2, 0.2), 0.1, 1.0)
    w_gate = centred(key_of[4], (EXPERTS, D, FF), D ** -0.5, 0.09375, ((0, 128), (2, 2)))
    w_up = centred(key_of[5], (EXPERTS, D, FF), D ** -0.5, 0.09375, ((0, 128), (2, 2)))
    w_down = centred(key_of[6], (EXPERTS, FF, D), FF ** -0.5, 0.1875, ((0, 128), (1, 2)))
    return {"tokens": tokens, "out_grad": out_grad, "route_ids": route_ids, "route_gates": route_gates, "w_gate": w_gate, "w_up": w_up, "w_down": w_down}


def reference(tokens, out_grad, route_ids, route_gates, w_gate, w_up, w_down):
    pair_total = TOKENS * TOP_WIN
    max_rows = N_EXPERT * CAP
    flat_ids = route_ids.reshape(-1).astype(jnp.int32)
    sorted_pairs = jnp.argsort(flat_ids, stable=True).astype(jnp.int32)
    expert_load = jnp.sum((flat_ids[:, None] == jnp.arange(EXPERTS, dtype=jnp.int32)[None, :]).astype(jnp.int32), axis=0)
    load_start = (jnp.cumsum(expert_load) - expert_load).astype(jnp.int32)
    padded_pairs = jnp.concatenate([sorted_pairs, jnp.zeros((max_rows,), jnp.int32)])
    flat_gates = route_gates.reshape(-1).astype(jnp.float32)

    def one_expert(carry, expert):
        grad_acc, score_acc = carry
        pair_idx = lax.dynamic_slice_in_dim(padded_pairs, load_start[expert], max_rows)
        valid = jnp.arange(max_rows, dtype=jnp.int32) < expert_load[expert]
        token_idx = pair_idx // TOP_WIN
        rows_x = tokens[token_idx]
        rows_d = out_grad[token_idx]
        gate_pre = jnp.dot(rows_x, w_gate[expert], preferred_element_type=jnp.float32)
        up_pre = jnp.dot(rows_x, w_up[expert], preferred_element_type=jnp.float32)
        grad_hidden = jnp.dot(rows_d, w_down[expert].T, preferred_element_type=jnp.float32)
        sigma_gate = jax.nn.sigmoid(gate_pre)
        act_gate = gate_pre * sigma_gate
        score = jnp.sum(act_gate * up_pre * grad_hidden, axis=1)
        grad_gate_pre = (grad_hidden * up_pre * sigma_gate * (1.0 + gate_pre * (1.0 - sigma_gate))).astype(jnp.bfloat16)
        grad_up_pre = (grad_hidden * act_gate).astype(jnp.bfloat16)
        pair_grad = (jnp.dot(grad_gate_pre, w_gate[expert].T, preferred_element_type=jnp.float32)
                     + jnp.dot(grad_up_pre, w_up[expert].T, preferred_element_type=jnp.float32)).astype(jnp.bfloat16)
        weighted = pair_grad.astype(jnp.float32) * flat_gates[pair_idx][:, None]
        safe_token = jnp.where(valid, token_idx, TOKENS)
        safe_pair = jnp.where(valid, pair_idx, pair_total)
        grad_acc = grad_acc.at[safe_token].add(weighted, mode="drop")
        score_acc = score_acc.at[safe_pair].set(score, mode="drop")
        return (grad_acc, score_acc), None

    start = (jnp.zeros((TOKENS, D), jnp.float32), jnp.zeros((pair_total,), jnp.float32))
    (grad_acc, score_acc), _ = lax.scan(one_expert, start, jnp.arange(EXPERTS, dtype=jnp.int32))
    token_grad = grad_acc.astype(jnp.bfloat16)
    gate_grad = score_acc.reshape(TOKENS, TOP_WIN).astype(jnp.bfloat16)
    return token_grad, gate_grad
```

```python
import jax
import jax.numpy as jnp
from jax import lax
from jax.sharding import PartitionSpec as P


def body(tokens, out_grad, route_ids, route_gates, w_gate, w_up, w_down):
    expert_count = lax.axis_size("expert")
    pair_count = lax.axis_size("hid")
    hid_idx = lax.axis_index("hid")
    tok_rows, model_width = tokens.shape
    top_count = route_ids.shape[1]
    capacity = 3 * tok_rows * top_count // (2 * expert_count)
    slot_count = expert_count * capacity
    half_width = model_width // pair_count
    pair_total = tok_rows * top_count
    flat_ids = route_ids.reshape(-1)
    one_hot = (flat_ids[:, None] == jnp.arange(expert_count, dtype=jnp.int32)[None, :]).astype(
        jnp.int32
    )
    earlier = jnp.cumsum(one_hot, axis=0) - one_hot
    slot_index = jnp.sum(earlier * one_hot, axis=1)
    dest_slot = flat_ids * capacity + slot_index
    slot_pair = jnp.zeros((slot_count,), jnp.int32).at[dest_slot].set(
        jnp.arange(pair_total, dtype=jnp.int32)
    )
    slot_token = slot_pair // top_count
    x_half = lax.dynamic_slice_in_dim(tokens, hid_idx * half_width, half_width, axis=1)
    d_half = lax.dynamic_slice_in_dim(out_grad, hid_idx * half_width, half_width, axis=1)
    send = jnp.stack([x_half[slot_token], d_half[slot_token]], axis=1).reshape(
        expert_count, capacity, 2, half_width
    )
    recv = lax.all_to_all(send, "expert", split_axis=0, concat_axis=0, tiled=True)
    full = lax.all_gather(recv, "hid", axis=3, tiled=True)
    rows_x = full[:, :, 0, :].reshape(slot_count, model_width)
    rows_d = full[:, :, 1, :].reshape(slot_count, model_width)
    gate_mat = w_gate[0]
    up_mat = w_up[0]
    down_mat = w_down[0]
    contract_last = (((1,), (1,)), ((), ()))
    gate_pre = jnp.dot(rows_x, gate_mat, preferred_element_type=jnp.float32)
    up_pre = jnp.dot(rows_x, up_mat, preferred_element_type=jnp.float32)
    grad_hidden = lax.dot_general(
        rows_d, down_mat, contract_last, preferred_element_type=jnp.float32
    )
    sigma_gate = jax.nn.sigmoid(gate_pre)
    act_gate = gate_pre * sigma_gate
    score_part = jnp.sum(act_gate * up_pre * grad_hidden, axis=1)
    grad_gate_pre = (
        grad_hidden * up_pre * sigma_gate * (1.0 + gate_pre * (1.0 - sigma_gate))
    ).astype(jnp.bfloat16)
    grad_up_pre = (grad_hidden * act_gate).astype(jnp.bfloat16)
    grad_part = lax.dot_general(
        grad_gate_pre, gate_mat, contract_last, preferred_element_type=jnp.float32
    ) + lax.dot_general(grad_up_pre, up_mat, contract_last, preferred_element_type=jnp.float32)
    grad_share = lax.psum_scatter(grad_part, "hid", scatter_dimension=1, tiled=True).astype(
        jnp.bfloat16
    )
    score_full = lax.psum(score_part, "hid").astype(jnp.bfloat16)
    back_grad, back_score = (
        lax.all_to_all(
            grad_share.reshape(expert_count, capacity, half_width),
            "expert",
            split_axis=0,
            concat_axis=0,
            tiled=True,
        ),
        lax.all_to_all(
            score_full.reshape(expert_count, capacity),
            "expert",
            split_axis=0,
            concat_axis=0,
            tiled=True,
        ),
    )
    picked = back_grad.reshape(slot_count, half_width)[dest_slot]
    picked = picked.reshape(tok_rows, top_count, half_width).astype(jnp.float32)
    token_grad = jnp.einsum("tkd,tk->td", picked, route_gates).astype(jnp.bfloat16)
    gate_grad = back_score.reshape(slot_count)[dest_slot].reshape(tok_rows, top_count)
    return (token_grad, gate_grad)


def solution(mesh):
    return jax.shard_map(
        body,
        mesh=mesh,
        in_specs=(
            P("expert", None),
            P("expert", None),
            P("expert", None),
            P("expert", None),
            P("expert", None, "hid"),
            P("expert", None, "hid"),
            P("expert", "hid", None),
        ),
        out_specs=(P("expert", "hid"), P("expert", None)),
        check_vma=False,
    )
```

```python
import jax
import jax.numpy as jnp
from jax import lax
from jax.sharding import PartitionSpec as P


def body(tokens, out_grad, route_ids, route_gates, w_gate, w_up, w_down):
    expert_count = lax.axis_size("expert")
    pair_count = lax.axis_size("hid")
    hid_idx = lax.axis_index("hid")
    tok_rows, model_width = tokens.shape
    top_count = route_ids.shape[1]
    capacity = 3 * tok_rows * top_count // (2 * expert_count)
    slot_count = expert_count * capacity
    half_width = model_width // pair_count
    pair_total = tok_rows * top_count
    flat_ids = route_ids.reshape(-1)
    one_hot = (flat_ids[:, None] == jnp.arange(expert_count, dtype=jnp.int32)[None, :]).astype(
        jnp.int32
    )
    earlier = jnp.cumsum(one_hot, axis=0) - one_hot
    slot_index = jnp.sum(earlier * one_hot, axis=1)
    dest_slot = flat_ids * capacity + slot_index
    slot_pair = jnp.zeros((slot_count,), jnp.int32).at[dest_slot].set(
        jnp.arange(pair_total, dtype=jnp.int32)
    )
    slot_token = slot_pair // top_count
    source = jnp.where(hid_idx == 0, tokens, out_grad)
    send = source[slot_token].reshape(expert_count, capacity // 2, 2, model_width)
    recv = lax.all_to_all(send, "expert", split_axis=0, concat_axis=0, tiled=True)
    both = lax.all_gather(recv, "hid", axis=0, tiled=False)
    rows_x = both[0].reshape(slot_count, model_width)
    rows_d = both[1].reshape(slot_count, model_width)
    gate_mat = w_gate[0]
    up_mat = w_up[0]
    down_mat = w_down[0]
    contract_last = (((1,), (1,)), ((), ()))
    gate_pre = jnp.dot(rows_x, gate_mat, preferred_element_type=jnp.float32)
    up_pre = jnp.dot(rows_x, up_mat, preferred_element_type=jnp.float32)
    grad_hidden = lax.dot_general(
        rows_d, down_mat, contract_last, preferred_element_type=jnp.float32
    )
    sigma_gate = jax.nn.sigmoid(gate_pre)
    act_gate = gate_pre * sigma_gate
    score_part = jnp.sum(act_gate * up_pre * grad_hidden, axis=1)
    grad_gate_pre = (
        grad_hidden * up_pre * sigma_gate * (1.0 + gate_pre * (1.0 - sigma_gate))
    ).astype(jnp.bfloat16)
    grad_up_pre = (grad_hidden * act_gate).astype(jnp.bfloat16)
    grad_part = lax.dot_general(
        grad_gate_pre, gate_mat, contract_last, preferred_element_type=jnp.float32
    ) + lax.dot_general(grad_up_pre, up_mat, contract_last, preferred_element_type=jnp.float32)
    grad_share = lax.psum_scatter(grad_part, "hid", scatter_dimension=1, tiled=True).astype(
        jnp.bfloat16
    )
    score_full = lax.psum(score_part, "hid").astype(jnp.bfloat16)
    score_cols = jnp.zeros((slot_count, 128), jnp.bfloat16).at[:, 0].set(score_full)
    back_send = jnp.concatenate([grad_share, score_cols], axis=1)
    back_width = back_send.shape[1]
    back = lax.all_to_all(
        back_send.reshape(expert_count, capacity // 2, 2, back_width),
        "expert",
        split_axis=0,
        concat_axis=0,
        tiled=True,
    ).reshape(slot_count, back_width)
    picked = back[dest_slot]
    pair_grad = picked[:, :half_width].reshape(tok_rows, top_count, half_width)
    token_grad = jnp.einsum(
        "tkd,tk->td", pair_grad.astype(jnp.float32), route_gates
    ).astype(jnp.bfloat16)
    gate_grad = picked[:, half_width].reshape(tok_rows, top_count)
    return (token_grad, gate_grad)


def solution(mesh):
    return jax.shard_map(
        body,
        mesh=mesh,
        in_specs=(
            P("expert", None),
            P("expert", None),
            P("expert", None),
            P("expert", None),
            P("expert", None, "hid"),
            P("expert", None, "hid"),
            P("expert", "hid", None),
        ),
        out_specs=(P("expert", "hid"), P("expert", None)),
        check_vma=False,
    )
```

```python
import jax
import jax.numpy as jnp
from jax import lax
from jax.sharding import PartitionSpec as P


def body(tokens, out_grad, route_ids, route_gates, w_gate, w_up, w_down):
    expert_count = lax.axis_size("expert")
    pair_count = lax.axis_size("hid")
    hid_idx = lax.axis_index("hid")
    tok_rows, model_width = tokens.shape
    top_count = route_ids.shape[1]
    capacity = 3 * tok_rows * top_count // (2 * expert_count)
    slot_count = expert_count * capacity
    half_width = model_width // pair_count
    pair_total = tok_rows * top_count
    flat_ids = route_ids.reshape(-1)
    one_hot = (flat_ids[:, None] == jnp.arange(expert_count, dtype=jnp.int32)[None, :]).astype(
        jnp.int32
    )
    earlier = jnp.cumsum(one_hot, axis=0) - one_hot
    slot_index = jnp.sum(earlier * one_hot, axis=1)
    dest_slot = flat_ids * capacity + slot_index
    slot_pair = jnp.zeros((slot_count,), jnp.int32).at[dest_slot].set(
        jnp.arange(pair_total, dtype=jnp.int32)
    )
    slot_token = slot_pair // top_count
    source = jnp.where(hid_idx == 0, tokens, out_grad)
    quad = (expert_count, capacity // 2, 2)
    send = source[slot_token.reshape(quad)]
    recv = lax.all_to_all(send, "expert", split_axis=0, concat_axis=0, tiled=True)
    both = lax.all_gather(recv, "hid", axis=0, tiled=False)
    rows_x = both[0]
    rows_d = both[1]
    gate_mat = w_gate[0]
    up_mat = w_up[0]
    down_mat = w_down[0]
    gate_pre = jnp.einsum("ejqc,cf->ejqf", rows_x, gate_mat, preferred_element_type=jnp.float32)
    up_pre = jnp.einsum("ejqc,cf->ejqf", rows_x, up_mat, preferred_element_type=jnp.float32)
    grad_hidden = jnp.einsum(
        "ejqc,fc->ejqf", rows_d, down_mat, preferred_element_type=jnp.float32
    )
    sigma_gate = jax.nn.sigmoid(gate_pre)
    act_gate = gate_pre * sigma_gate
    score_part = jnp.sum(act_gate * up_pre * grad_hidden, axis=3)
    grad_gate_pre = (
        grad_hidden * up_pre * sigma_gate * (1.0 + gate_pre * (1.0 - sigma_gate))
    ).astype(jnp.bfloat16)
    grad_up_pre = (grad_hidden * act_gate).astype(jnp.bfloat16)
    grad_part = jnp.einsum(
        "ejqf,cf->ejqc", grad_gate_pre, gate_mat, preferred_element_type=jnp.float32
    ) + jnp.einsum("ejqf,cf->ejqc", grad_up_pre, up_mat, preferred_element_type=jnp.float32)
    grad_share = lax.psum_scatter(grad_part, "hid", scatter_dimension=3, tiled=True).astype(
        jnp.bfloat16
    )
    score_full = lax.psum(score_part, "hid").astype(jnp.bfloat16)
    score_cols = jnp.zeros(quad + (128,), jnp.bfloat16).at[..., 0].set(score_full)
    back_send = jnp.concatenate([grad_share, score_cols], axis=3)
    back = lax.all_to_all(back_send, "expert", split_axis=0, concat_axis=0, tiled=True)
    picked = back[flat_ids, slot_index // 2, slot_index % 2]
    pair_grad = picked[:, :half_width].reshape(tok_rows, top_count, half_width)
    token_grad = jnp.sum(
        pair_grad.astype(jnp.float32) * route_gates[:, :, None], axis=1
    ).astype(jnp.bfloat16)
    gate_grad = picked[:, half_width].reshape(tok_rows, top_count)
    return (token_grad, gate_grad)


def solution(mesh):
    return jax.shard_map(
        body,
        mesh=mesh,
        in_specs=(
            P("expert", None),
            P("expert", None),
            P("expert", None),
            P("expert", None),
            P("expert", None, "hid"),
            P("expert", None, "hid"),
            P("expert", "hid", None),
        ),
        out_specs=(P("expert", "hid"), P("expert", None)),
        check_vma=False,
    )
```

```python
import jax
import jax.numpy as jnp
from jax import lax
from jax.sharding import PartitionSpec as P


def body(tokens, out_grad, route_ids, route_gates, w_gate, w_up, w_down):
    expert_count = lax.axis_size("expert")
    pair_count = lax.axis_size("hid")
    hid_idx = lax.axis_index("hid")
    tok_rows, model_width = tokens.shape
    top_count = route_ids.shape[1]
    capacity = 3 * tok_rows * top_count // (2 * expert_count)
    slot_count = expert_count * capacity
    half_width = model_width // pair_count
    pair_total = tok_rows * top_count
    gate_full = lax.all_gather(w_gate[0], "hid", axis=1, tiled=True)
    up_full = lax.all_gather(w_up[0], "hid", axis=1, tiled=True)
    down_full = lax.all_gather(w_down[0], "hid", axis=0, tiled=True)
    flat_ids = route_ids.reshape(-1)
    one_hot = (flat_ids[:, None] == jnp.arange(expert_count, dtype=jnp.int32)[None, :]).astype(
        jnp.int32
    )
    earlier = jnp.cumsum(one_hot, axis=0) - one_hot
    slot_index = jnp.sum(earlier * one_hot, axis=1)
    dest_slot = flat_ids * capacity + slot_index
    slot_pair = jnp.zeros((slot_count,), jnp.int32).at[dest_slot].set(
        jnp.arange(pair_total, dtype=jnp.int32)
    )
    slot_token = slot_pair // top_count
    half_cap = capacity // pair_count
    own_token = lax.dynamic_index_in_dim(
        slot_token.reshape(expert_count, half_cap, pair_count), hid_idx, axis=2, keepdims=False
    )
    source = jnp.stack([tokens, out_grad])
    kind = jnp.broadcast_to(jnp.arange(2, dtype=jnp.int32), (expert_count, half_cap, 2))
    send = source[kind, jnp.broadcast_to(own_token[:, :, None], kind.shape)]
    recv = lax.all_to_all(send, "expert", split_axis=0, concat_axis=0, tiled=True)
    rows_x = recv[:, :, 0]
    rows_d = recv[:, :, 1]
    gate_pre = jnp.einsum("ejc,cf->ejf", rows_x, gate_full, preferred_element_type=jnp.float32)
    up_pre = jnp.einsum("ejc,cf->ejf", rows_x, up_full, preferred_element_type=jnp.float32)
    grad_hidden = jnp.einsum(
        "ejc,fc->ejf", rows_d, down_full, preferred_element_type=jnp.float32
    )
    sigma_gate = jax.nn.sigmoid(gate_pre)
    act_gate = gate_pre * sigma_gate
    score = jnp.sum(act_gate * up_pre * grad_hidden, axis=2).astype(jnp.bfloat16)
    grad_gate_pre = (
        grad_hidden * up_pre * sigma_gate * (1.0 + gate_pre * (1.0 - sigma_gate))
    ).astype(jnp.bfloat16)
    grad_up_pre = (grad_hidden * act_gate).astype(jnp.bfloat16)
    pair_grad = (
        jnp.einsum("ejf,cf->ejc", grad_gate_pre, gate_full, preferred_element_type=jnp.float32)
        + jnp.einsum("ejf,cf->ejc", grad_up_pre, up_full, preferred_element_type=jnp.float32)
    ).astype(jnp.bfloat16)
    score_cols = jnp.zeros((expert_count, half_cap, pair_count, 128), jnp.bfloat16)
    score_cols = score_cols.at[..., 0].set(score[:, :, None])
    back_send = jnp.concatenate(
        [pair_grad.reshape(expert_count, half_cap, pair_count, half_width), score_cols], axis=3
    )
    back = lax.all_to_all(back_send, "expert", split_axis=0, concat_axis=0, tiled=True)
    picked = back[flat_ids, slot_index // pair_count]
    mine = (slot_index % pair_count) == hid_idx
    weight = jnp.where(mine, route_gates.reshape(-1), 0.0)
    grads = picked[:, :, :half_width].reshape(tok_rows, top_count, model_width)
    partial = jnp.sum(
        grads.astype(jnp.float32) * weight.reshape(tok_rows, top_count, 1), axis=1
    )
    token_grad = lax.psum_scatter(partial, "hid", scatter_dimension=1, tiled=True).astype(
        jnp.bfloat16
    )
    own_score = jnp.where(mine, picked[:, 0, half_width].astype(jnp.float32), 0.0)
    gate_grad = lax.psum(own_score, "hid").astype(jnp.bfloat16).reshape(tok_rows, top_count)
    return (token_grad, gate_grad)


def solution(mesh):
    return jax.shard_map(
        body,
        mesh=mesh,
        in_specs=(
            P("expert", None),
            P("expert", None),
            P("expert", None),
            P("expert", None),
            P("expert", None, "hid"),
            P("expert", None, "hid"),
            P("expert", "hid", None),
        ),
        out_specs=(P("expert", "hid"), P("expert", None)),
        check_vma=False,
    )
```

```python
import jax
import jax.numpy as jnp
from jax import lax
from jax.sharding import PartitionSpec as P


def body(tokens, out_grad, route_ids, route_gates, w_gate, w_up, w_down):
    expert_count = lax.axis_size("expert")
    pair_count = lax.axis_size("hid")
    hid_idx = lax.axis_index("hid")
    tok_rows, model_width = tokens.shape
    top_count = route_ids.shape[1]
    capacity = 3 * tok_rows * top_count // (2 * expert_count)
    slot_count = expert_count * capacity
    half_width = model_width // pair_count
    pair_total = tok_rows * top_count
    gate_full = lax.all_gather(w_gate[0], "hid", axis=1, tiled=True)
    up_full = lax.all_gather(w_up[0], "hid", axis=1, tiled=True)
    down_full = lax.all_gather(w_down[0], "hid", axis=0, tiled=True)
    flat_ids = route_ids.reshape(-1)
    one_hot = (flat_ids[:, None] == jnp.arange(expert_count, dtype=jnp.int32)[None, :]).astype(
        jnp.int32
    )
    earlier = jnp.cumsum(one_hot, axis=0) - one_hot
    slot_index = jnp.sum(earlier * one_hot, axis=1)
    dest_slot = flat_ids * capacity + slot_index
    slot_pair = jnp.zeros((slot_count,), jnp.int32).at[dest_slot].set(
        jnp.arange(pair_total, dtype=jnp.int32)
    )
    slot_token = slot_pair // top_count
    half_cap = capacity // pair_count
    own_token = lax.dynamic_index_in_dim(
        slot_token.reshape(expert_count, half_cap, pair_count), hid_idx, axis=2, keepdims=False
    )
    rows_of = own_token.T
    send = jnp.stack([tokens[rows_of], out_grad[rows_of]]).transpose(2, 1, 0, 3)
    recv = lax.all_to_all(send, "expert", split_axis=0, concat_axis=0, tiled=True)
    by_kind = recv.transpose(2, 1, 0, 3).reshape(2, expert_count * half_cap, model_width)
    rows_x = by_kind[0]
    rows_d = by_kind[1]
    gate_pre = jnp.dot(rows_x, gate_full, preferred_element_type=jnp.float32)
    up_pre = jnp.dot(rows_x, up_full, preferred_element_type=jnp.float32)
    contract_last = (((1,), (1,)), ((), ()))
    grad_hidden = lax.dot_general(
        rows_d, down_full, contract_last, preferred_element_type=jnp.float32
    )
    sigma_gate = jax.nn.sigmoid(gate_pre)
    act_gate = gate_pre * sigma_gate
    score = jnp.sum(act_gate * up_pre * grad_hidden, axis=1).astype(jnp.bfloat16)
    grad_gate_pre = (
        grad_hidden * up_pre * sigma_gate * (1.0 + gate_pre * (1.0 - sigma_gate))
    ).astype(jnp.bfloat16)
    grad_up_pre = (grad_hidden * act_gate).astype(jnp.bfloat16)
    pair_grad = (
        lax.dot_general(grad_gate_pre, gate_full, contract_last, preferred_element_type=jnp.float32)
        + lax.dot_general(grad_up_pre, up_full, contract_last, preferred_element_type=jnp.float32)
    ).astype(jnp.bfloat16)
    pair_grad = pair_grad.reshape(half_cap, expert_count, pair_count, half_width)
    score_cols = jnp.zeros((half_cap, expert_count, pair_count, 128), jnp.bfloat16)
    score_cols = score_cols.at[..., 0].set(score.reshape(half_cap, expert_count, 1))
    back_send = jnp.concatenate([pair_grad, score_cols], axis=3).transpose(1, 0, 2, 3)
    back = lax.all_to_all(back_send, "expert", split_axis=0, concat_axis=0, tiled=True)
    mine = (slot_index % pair_count) == hid_idx
    weight = jnp.where(mine, route_gates.reshape(-1), 0.0)
    own_slot = flat_ids * half_cap + slot_index // pair_count
    token_of_pair = jnp.arange(pair_total, dtype=jnp.int32) // top_count
    gate_matrix = jnp.zeros((tok_rows, expert_count * half_cap), jnp.float32).at[
        token_of_pair, own_slot
    ].add(weight)
    back_rows = back.reshape(expert_count * half_cap, pair_count, back.shape[3])
    partial = jnp.einsum(
        "ts,shc->thc",
        gate_matrix,
        back_rows[:, :, :half_width].astype(jnp.float32),
        precision=lax.Precision.HIGHEST,
    ).reshape(tok_rows, model_width)
    token_grad = lax.psum_scatter(partial, "hid", scatter_dimension=1, tiled=True).astype(
        jnp.bfloat16
    )
    picked_score = back_rows[:, 0, half_width][own_slot]
    own_score = jnp.where(mine, picked_score.astype(jnp.float32), 0.0)
    gate_grad = lax.psum(own_score, "hid").astype(jnp.bfloat16).reshape(tok_rows, top_count)
    return (token_grad, gate_grad)


def solution(mesh):
    return jax.shard_map(
        body,
        mesh=mesh,
        in_specs=(
            P("expert", None),
            P("expert", None),
            P("expert", None),
            P("expert", None),
            P("expert", None, "hid"),
            P("expert", None, "hid"),
            P("expert", "hid", None),
        ),
        out_specs=(P("expert", "hid"), P("expert", None)),
        check_vma=False,
    )
```

```python
import jax
import jax.numpy as jnp
from jax import lax
from jax.sharding import PartitionSpec as P


def body(tokens, out_grad, route_ids, route_gates, w_gate, w_up, w_down):
    expert_count = lax.axis_size("expert")
    pair_count = lax.axis_size("hid")
    hid_idx = lax.axis_index("hid")
    tok_rows, model_width = tokens.shape
    top_count = route_ids.shape[1]
    capacity = 3 * tok_rows * top_count // (2 * expert_count)
    slot_count = expert_count * capacity
    half_width = model_width // pair_count
    pair_total = tok_rows * top_count
    flat_ids = route_ids.reshape(-1)
    one_hot = (flat_ids[:, None] == jnp.arange(expert_count, dtype=jnp.int32)[None, :]).astype(
        jnp.int32
    )
    earlier = jnp.cumsum(one_hot, axis=0) - one_hot
    slot_index = jnp.sum(earlier * one_hot, axis=1)
    dest_slot = flat_ids * capacity + slot_index
    slot_pair = jnp.zeros((slot_count,), jnp.int32).at[dest_slot].set(
        jnp.arange(pair_total, dtype=jnp.int32)
    )
    slot_token = slot_pair // top_count
    source = jnp.where(hid_idx == 0, tokens, out_grad)
    quad = (expert_count, capacity // 2, 2)
    send = source[slot_token.reshape(quad)]
    recv = lax.all_to_all(send, "expert", split_axis=0, concat_axis=0, tiled=True)
    both = lax.all_gather(recv, "hid", axis=0, tiled=False)
    rows_x = both[0]
    rows_d = both[1]
    gate_mat = w_gate[0]
    up_mat = w_up[0]
    down_mat = w_down[0]
    gate_pre = jnp.einsum("ejqc,cf->ejqf", rows_x, gate_mat, preferred_element_type=jnp.float32)
    up_pre = jnp.einsum("ejqc,cf->ejqf", rows_x, up_mat, preferred_element_type=jnp.float32)
    grad_hidden = jnp.einsum(
        "ejqc,fc->ejqf", rows_d, down_mat, preferred_element_type=jnp.float32
    )
    sigma_gate = jax.nn.sigmoid(gate_pre)
    act_gate = gate_pre * sigma_gate
    score_part = jnp.sum(act_gate * up_pre * grad_hidden, axis=3)
    grad_gate_pre = (
        grad_hidden * up_pre * sigma_gate * (1.0 + gate_pre * (1.0 - sigma_gate))
    ).astype(jnp.bfloat16)
    grad_up_pre = (grad_hidden * act_gate).astype(jnp.bfloat16)
    grad_part = jnp.einsum(
        "ejqf,cf->ejqc", grad_gate_pre, gate_mat, preferred_element_type=jnp.float32
    ) + jnp.einsum("ejqf,cf->ejqc", grad_up_pre, up_mat, preferred_element_type=jnp.float32)
    grad_share = lax.psum_scatter(
        grad_part.astype(jnp.bfloat16), "hid", scatter_dimension=3, tiled=True
    )
    score_full = lax.psum(score_part, "hid").astype(jnp.bfloat16)
    score_cols = jnp.zeros(quad + (128,), jnp.bfloat16).at[..., 0].set(score_full)
    back_send = jnp.concatenate([grad_share, score_cols], axis=3)
    back = lax.all_to_all(back_send, "expert", split_axis=0, concat_axis=0, tiled=True)
    route_slot = slot_index.reshape(tok_rows, top_count)
    token_grad = jnp.zeros((tok_rows, half_width), jnp.float32)
    scores = []
    for k in range(top_count):
        row = back[route_ids[:, k], route_slot[:, k] // 2, route_slot[:, k] % 2]
        token_grad = token_grad + row[:, :half_width].astype(jnp.float32) * route_gates[:, k, None]
        scores.append(row[:, half_width])
    token_grad = token_grad.astype(jnp.bfloat16)
    gate_grad = jnp.stack(scores, axis=1)
    return (token_grad, gate_grad)


def solution(mesh):
    return jax.shard_map(
        body,
        mesh=mesh,
        in_specs=(
            P("expert", None),
            P("expert", None),
            P("expert", None),
            P("expert", None),
            P("expert", None, "hid"),
            P("expert", None, "hid"),
            P("expert", "hid", None),
        ),
        out_specs=(P("expert", "hid"), P("expert", None)),
        check_vma=False,
    )
```

```python
import jax
import jax.numpy as jnp
from jax import lax
from jax.sharding import PartitionSpec as P


def body(tokens, out_grad, route_ids, route_gates, w_gate, w_up, w_down):
    expert_count = lax.axis_size("expert")
    pair_count = lax.axis_size("hid")
    hid_idx = lax.axis_index("hid")
    tok_rows, model_width = tokens.shape
    top_count = route_ids.shape[1]
    capacity = 3 * tok_rows * top_count // (2 * expert_count)
    slot_count = expert_count * capacity
    half_width = model_width // pair_count
    pair_total = tok_rows * top_count
    flat_ids = route_ids.reshape(-1)
    one_hot = (flat_ids[:, None] == jnp.arange(expert_count, dtype=jnp.int32)[None, :]).astype(
        jnp.int32
    )
    earlier = jnp.cumsum(one_hot, axis=0) - one_hot
    slot_index = jnp.sum(earlier * one_hot, axis=1)
    dest_slot = flat_ids * capacity + slot_index
    slot_pair = jnp.zeros((slot_count,), jnp.int32).at[dest_slot].set(
        jnp.arange(pair_total, dtype=jnp.int32)
    )
    slot_token = slot_pair // top_count
    source = jnp.where(hid_idx == 0, tokens, out_grad)
    quad = (expert_count, capacity // 2, 2)
    send = source[slot_token.reshape(quad)]
    recv = lax.all_to_all(send, "expert", split_axis=0, concat_axis=0, tiled=True)
    swap = [(0, 1), (1, 0)]
    other = lax.ppermute(recv, "hid", swap)
    first = hid_idx == 0
    rows_x = jnp.where(first, recv, other)
    rows_d = jnp.where(first, other, recv)
    gate_mat = w_gate[0]
    up_mat = w_up[0]
    down_mat = w_down[0]
    gate_pre = jnp.einsum("ejqc,cf->ejqf", rows_x, gate_mat, preferred_element_type=jnp.float32)
    up_pre = jnp.einsum("ejqc,cf->ejqf", rows_x, up_mat, preferred_element_type=jnp.float32)
    grad_hidden = jnp.einsum(
        "ejqc,fc->ejqf", rows_d, down_mat, preferred_element_type=jnp.float32
    )
    sigma_gate = jax.nn.sigmoid(gate_pre)
    act_gate = gate_pre * sigma_gate
    score_part = jnp.sum(act_gate * up_pre * grad_hidden, axis=3)
    grad_gate_pre = (
        grad_hidden * up_pre * sigma_gate * (1.0 + gate_pre * (1.0 - sigma_gate))
    ).astype(jnp.bfloat16)
    grad_up_pre = (grad_hidden * act_gate).astype(jnp.bfloat16)
    grad_part = jnp.einsum(
        "ejqf,cf->ejqc", grad_gate_pre, gate_mat, preferred_element_type=jnp.float32
    ) + jnp.einsum("ejqf,cf->ejqc", grad_up_pre, up_mat, preferred_element_type=jnp.float32)
    own_half = lax.dynamic_slice_in_dim(grad_part, hid_idx * half_width, half_width, axis=3)
    give_half = lax.dynamic_slice_in_dim(
        grad_part, (1 - hid_idx) * half_width, half_width, axis=3
    ).astype(jnp.bfloat16)
    got_half = lax.ppermute(give_half, "hid", swap)
    grad_share = (
        own_half.astype(jnp.bfloat16).astype(jnp.float32) + got_half.astype(jnp.float32)
    ).astype(jnp.bfloat16)
    score_full = lax.psum(score_part, "hid").astype(jnp.bfloat16)
    score_cols = jnp.zeros(quad + (128,), jnp.bfloat16).at[..., 0].set(score_full)
    back_send = jnp.concatenate([grad_share, score_cols], axis=3)
    back = lax.all_to_all(back_send, "expert", split_axis=0, concat_axis=0, tiled=True)
    route_slot = slot_index.reshape(tok_rows, top_count)
    token_grad = jnp.zeros((tok_rows, half_width), jnp.float32)
    scores = []
    for k in range(top_count):
        row = back[route_ids[:, k], route_slot[:, k] // 2, route_slot[:, k] % 2]
        token_grad = token_grad + row[:, :half_width].astype(jnp.float32) * route_gates[:, k, None]
        scores.append(row[:, half_width])
    token_grad = token_grad.astype(jnp.bfloat16)
    gate_grad = jnp.stack(scores, axis=1)
    return (token_grad, gate_grad)


def solution(mesh):
    return jax.shard_map(
        body,
        mesh=mesh,
        in_specs=(
            P("expert", None),
            P("expert", None),
            P("expert", None),
            P("expert", None),
            P("expert", None, "hid"),
            P("expert", None, "hid"),
            P("expert", "hid", None),
        ),
        out_specs=(P("expert", "hid"), P("expert", None)),
        check_vma=False,
    )
```

```python
import jax
import jax.numpy as jnp
from jax import lax
from jax.sharding import PartitionSpec as P


def body(tokens, out_grad, route_ids, route_gates, w_gate, w_up, w_down):
    expert_count = lax.axis_size("expert")
    pair_count = lax.axis_size("hid")
    hid_idx = lax.axis_index("hid")
    tok_rows, model_width = tokens.shape
    top_count = route_ids.shape[1]
    capacity = 3 * tok_rows * top_count // (2 * expert_count)
    slot_count = expert_count * capacity
    half_width = model_width // pair_count
    pair_total = tok_rows * top_count
    flat_ids = route_ids.reshape(-1)
    one_hot = (flat_ids[:, None] == jnp.arange(expert_count, dtype=jnp.int32)[None, :]).astype(
        jnp.int32
    )
    earlier = jnp.cumsum(one_hot, axis=0) - one_hot
    slot_index = jnp.sum(earlier * one_hot, axis=1)
    dest_slot = flat_ids * capacity + slot_index
    slot_pair = jnp.zeros((slot_count,), jnp.int32).at[dest_slot].set(
        jnp.arange(pair_total, dtype=jnp.int32)
    )
    slot_token = slot_pair // top_count
    source = jnp.where(hid_idx == 0, tokens, out_grad)
    quad = (expert_count, capacity // 2, 2)
    send = source[slot_token.reshape(quad)]
    recv = lax.all_to_all(send, "expert", split_axis=0, concat_axis=0, tiled=True)
    swap = [(0, 1), (1, 0)]
    other = lax.ppermute(recv, "hid", swap)
    first = hid_idx == 0
    gate_mat = w_gate[0]
    up_mat = w_up[0]
    down_mat = w_down[0]

    def expert_math(rows_x, rows_d):
        gate_pre = jnp.einsum(
            "ejqc,cf->ejqf", rows_x, gate_mat, preferred_element_type=jnp.float32
        )
        up_pre = jnp.einsum("ejqc,cf->ejqf", rows_x, up_mat, preferred_element_type=jnp.float32)
        grad_hidden = jnp.einsum(
            "ejqc,fc->ejqf", rows_d, down_mat, preferred_element_type=jnp.float32
        )
        sigma_gate = jax.nn.sigmoid(gate_pre)
        act_gate = gate_pre * sigma_gate
        score_part = jnp.sum(act_gate * up_pre * grad_hidden, axis=3)
        grad_gate_pre = (
            grad_hidden * up_pre * sigma_gate * (1.0 + gate_pre * (1.0 - sigma_gate))
        ).astype(jnp.bfloat16)
        grad_up_pre = (grad_hidden * act_gate).astype(jnp.bfloat16)
        grad_part = jnp.einsum(
            "ejqf,cf->ejqc", grad_gate_pre, gate_mat, preferred_element_type=jnp.float32
        ) + jnp.einsum(
            "ejqf,cf->ejqc", grad_up_pre, up_mat, preferred_element_type=jnp.float32
        )
        return score_part, grad_part

    score_part, grad_part = lax.cond(
        first, expert_math, lambda a, b: expert_math(b, a), recv, other
    )
    own_half = lax.dynamic_slice_in_dim(grad_part, hid_idx * half_width, half_width, axis=3)
    give_half = lax.dynamic_slice_in_dim(
        grad_part, (1 - hid_idx) * half_width, half_width, axis=3
    ).astype(jnp.bfloat16)
    got_half = lax.ppermute(give_half, "hid", swap)
    grad_share = (
        own_half.astype(jnp.bfloat16).astype(jnp.float32) + got_half.astype(jnp.float32)
    ).astype(jnp.bfloat16)
    score_full = (score_part + lax.ppermute(score_part, "hid", swap)).astype(jnp.bfloat16)
    score_cols = jnp.zeros(quad + (128,), jnp.bfloat16).at[..., 0].set(score_full)
    back_send = jnp.concatenate([grad_share, score_cols], axis=3)
    back = lax.all_to_all(back_send, "expert", split_axis=0, concat_axis=0, tiled=True)
    route_slot = slot_index.reshape(tok_rows, top_count)
    token_grad = jnp.zeros((tok_rows, half_width), jnp.float32)
    scores = []
    for k in range(top_count):
        row = back[route_ids[:, k], route_slot[:, k] // 2, route_slot[:, k] % 2]
        token_grad = token_grad + row[:, :half_width].astype(jnp.float32) * route_gates[:, k, None]
        scores.append(row[:, half_width])
    token_grad = token_grad.astype(jnp.bfloat16)
    gate_grad = jnp.stack(scores, axis=1)
    return (token_grad, gate_grad)


def solution(mesh):
    return jax.shard_map(
        body,
        mesh=mesh,
        in_specs=(
            P("expert", None),
            P("expert", None),
            P("expert", None),
            P("expert", None),
            P("expert", None, "hid"),
            P("expert", None, "hid"),
            P("expert", "hid", None),
        ),
        out_specs=(P("expert", "hid"), P("expert", None)),
        check_vma=False,
    )
```

```python
import jax
import jax.numpy as jnp
from jax import lax
from jax.sharding import PartitionSpec as P


def body(tokens, out_grad, route_ids, route_gates, w_gate, w_up, w_down):
    expert_count = lax.axis_size("expert")
    pair_count = lax.axis_size("hid")
    hid_idx = lax.axis_index("hid")
    tok_rows, model_width = tokens.shape
    top_count = route_ids.shape[1]
    capacity = 3 * tok_rows * top_count // (2 * expert_count)
    slot_count = expert_count * capacity
    half_width = model_width // pair_count
    pair_total = tok_rows * top_count
    flat_ids = route_ids.reshape(-1)
    one_hot = (flat_ids[:, None] == jnp.arange(expert_count, dtype=jnp.int32)[None, :]).astype(
        jnp.int32
    )
    earlier = jnp.cumsum(one_hot, axis=0) - one_hot
    slot_index = jnp.sum(earlier * one_hot, axis=1)
    dest_slot = flat_ids * capacity + slot_index
    slot_pair = jnp.zeros((slot_count,), jnp.int32).at[dest_slot].set(
        jnp.arange(pair_total, dtype=jnp.int32)
    )
    slot_token = slot_pair // top_count
    source = jnp.where(hid_idx == 0, tokens, out_grad)
    quad = (expert_count, capacity // 2, 2)
    send = source[slot_token.reshape(quad)]
    recv = lax.all_to_all(send, "expert", split_axis=0, concat_axis=0, tiled=True)
    swap = [(0, 1), (1, 0)]
    other = lax.ppermute(recv, "hid", swap)
    first = hid_idx == 0
    rows_x = jnp.where(first, recv, other)
    rows_d = jnp.where(first, other, recv)
    gate_mat = w_gate[0]
    up_mat = w_up[0]
    down_mat = w_down[0]
    gate_pre = jnp.einsum("ejqc,cf->ejqf", rows_x, gate_mat, preferred_element_type=jnp.float32)
    up_pre = jnp.einsum("ejqc,cf->ejqf", rows_x, up_mat, preferred_element_type=jnp.float32)
    grad_hidden = jnp.einsum(
        "ejqc,fc->ejqf", rows_d, down_mat, preferred_element_type=jnp.float32
    )
    sigma_gate = jax.nn.sigmoid(gate_pre)
    act_gate = gate_pre * sigma_gate
    score_part = jnp.sum(act_gate * up_pre * grad_hidden, axis=3)
    grad_gate_pre = (
        grad_hidden * up_pre * sigma_gate * (1.0 + gate_pre * (1.0 - sigma_gate))
    ).astype(jnp.bfloat16)
    grad_up_pre = (grad_hidden * act_gate).astype(jnp.bfloat16)
    grad_part = jnp.einsum(
        "ejqf,cf->ejqc", grad_gate_pre, gate_mat, preferred_element_type=jnp.float32
    ) + jnp.einsum("ejqf,cf->ejqc", grad_up_pre, up_mat, preferred_element_type=jnp.float32)
    own_half = lax.dynamic_slice_in_dim(grad_part, hid_idx * half_width, half_width, axis=3)
    give_half = lax.dynamic_slice_in_dim(
        grad_part, (1 - hid_idx) * half_width, half_width, axis=3
    ).astype(jnp.bfloat16)
    got_half = lax.ppermute(give_half, "hid", swap)
    grad_share = (
        own_half.astype(jnp.bfloat16).astype(jnp.float32) + got_half.astype(jnp.float32)
    ).astype(jnp.bfloat16)
    score_full = (score_part + lax.ppermute(score_part, "hid", swap)).astype(jnp.bfloat16)
    score_cols = jnp.zeros(quad + (128,), jnp.bfloat16).at[..., 0].set(score_full)
    back_send = jnp.concatenate([grad_share, score_cols], axis=3)
    back = lax.all_to_all(back_send, "expert", split_axis=0, concat_axis=0, tiled=True)
    route_slot = slot_index.reshape(tok_rows, top_count)
    token_grad = jnp.zeros((tok_rows, half_width), jnp.float32)
    scores = []
    for k in range(top_count):
        row = back[route_ids[:, k], route_slot[:, k] // 2, route_slot[:, k] % 2]
        token_grad = token_grad + row[:, :half_width].astype(jnp.float32) * route_gates[:, k, None]
        scores.append(row[:, half_width])
    token_grad = token_grad.astype(jnp.bfloat16)
    gate_grad = jnp.stack(scores, axis=1)
    return (token_grad, gate_grad)


def solution(mesh):
    return jax.shard_map(
        body,
        mesh=mesh,
        in_specs=(
            P("expert", None),
            P("expert", None),
            P("expert", None),
            P("expert", None),
            P("expert", None, "hid"),
            P("expert", None, "hid"),
            P("expert", "hid", None),
        ),
        out_specs=(P("expert", "hid"), P("expert", None)),
        check_vma=False,
    )
```

```python
import jax
import jax.numpy as jnp
from jax import lax
from jax.sharding import PartitionSpec as P


def body(tokens, out_grad, route_ids, route_gates, w_gate, w_up, w_down):
    expert_count = lax.axis_size("expert")
    pair_count = lax.axis_size("hid")
    hid_idx = lax.axis_index("hid")
    tok_rows, model_width = tokens.shape
    top_count = route_ids.shape[1]
    capacity = 3 * tok_rows * top_count // (2 * expert_count)
    slot_count = expert_count * capacity
    half_width = model_width // pair_count
    pair_total = tok_rows * top_count
    flat_ids = route_ids.reshape(-1)
    one_hot = (flat_ids[:, None] == jnp.arange(expert_count, dtype=jnp.int32)[None, :]).astype(
        jnp.int32
    )
    earlier = jnp.cumsum(one_hot, axis=0) - one_hot
    slot_index = jnp.sum(earlier * one_hot, axis=1)
    dest_slot = flat_ids * capacity + slot_index
    slot_pair = jnp.zeros((slot_count,), jnp.int32).at[dest_slot].set(
        jnp.arange(pair_total, dtype=jnp.int32)
    )
    slot_token = slot_pair // top_count
    source = jnp.where(hid_idx == 0, tokens, out_grad)
    quad = (expert_count, capacity // 2, 2)
    pick = (
        slot_token.reshape(quad)[..., None] == jnp.arange(tok_rows, dtype=jnp.int32)
    ).astype(jnp.bfloat16)
    send = jnp.einsum(
        "ejqt,tc->ejqc", pick, source, preferred_element_type=jnp.float32
    ).astype(jnp.bfloat16)
    recv = lax.all_to_all(send, "expert", split_axis=0, concat_axis=0, tiled=True)
    swap = [(0, 1), (1, 0)]
    other = lax.ppermute(recv, "hid", swap)
    first = hid_idx == 0
    rows_x = jnp.where(first, recv, other)
    rows_d = jnp.where(first, other, recv)
    gate_mat = w_gate[0]
    up_mat = w_up[0]
    down_mat = w_down[0]
    gate_pre = jnp.einsum("ejqc,cf->ejqf", rows_x, gate_mat, preferred_element_type=jnp.float32)
    up_pre = jnp.einsum("ejqc,cf->ejqf", rows_x, up_mat, preferred_element_type=jnp.float32)
    grad_hidden = jnp.einsum(
        "ejqc,fc->ejqf", rows_d, down_mat, preferred_element_type=jnp.float32
    )
    sigma_gate = jax.nn.sigmoid(gate_pre)
    act_gate = gate_pre * sigma_gate
    score_part = jnp.sum(act_gate * up_pre * grad_hidden, axis=3)
    grad_gate_pre = (
        grad_hidden * up_pre * sigma_gate * (1.0 + gate_pre * (1.0 - sigma_gate))
    ).astype(jnp.bfloat16)
    grad_up_pre = (grad_hidden * act_gate).astype(jnp.bfloat16)
    grad_part = jnp.einsum(
        "ejqf,cf->ejqc", grad_gate_pre, gate_mat, preferred_element_type=jnp.float32
    ) + jnp.einsum("ejqf,cf->ejqc", grad_up_pre, up_mat, preferred_element_type=jnp.float32)
    own_half = lax.dynamic_slice_in_dim(grad_part, hid_idx * half_width, half_width, axis=3)
    give_half = lax.dynamic_slice_in_dim(
        grad_part, (1 - hid_idx) * half_width, half_width, axis=3
    ).astype(jnp.bfloat16)
    got_half = lax.ppermute(give_half, "hid", swap)
    grad_share = (
        own_half.astype(jnp.bfloat16).astype(jnp.float32) + got_half.astype(jnp.float32)
    ).astype(jnp.bfloat16)
    score_full = (score_part + lax.ppermute(score_part, "hid", swap)).astype(jnp.bfloat16)
    score_cols = jnp.zeros(quad + (128,), jnp.bfloat16).at[..., 0].set(score_full)
    back_send = jnp.concatenate([grad_share, score_cols], axis=3)
    back = lax.all_to_all(back_send, "expert", split_axis=0, concat_axis=0, tiled=True)
    route_slot = slot_index.reshape(tok_rows, top_count)
    token_grad = jnp.zeros((tok_rows, half_width), jnp.float32)
    scores = []
    for k in range(top_count):
        row = back[route_ids[:, k], route_slot[:, k] // 2, route_slot[:, k] % 2]
        token_grad = token_grad + row[:, :half_width].astype(jnp.float32) * route_gates[:, k, None]
        scores.append(row[:, half_width])
    token_grad = token_grad.astype(jnp.bfloat16)
    gate_grad = jnp.stack(scores, axis=1)
    return (token_grad, gate_grad)


def solution(mesh):
    return jax.shard_map(
        body,
        mesh=mesh,
        in_specs=(
            P("expert", None),
            P("expert", None),
            P("expert", None),
            P("expert", None),
            P("expert", None, "hid"),
            P("expert", None, "hid"),
            P("expert", "hid", None),
        ),
        out_specs=(P("expert", "hid"), P("expert", None)),
        check_vma=False,
    )
```

```python
import jax
import jax.numpy as jnp
from jax import lax
from jax.sharding import PartitionSpec as P


def body(tokens, out_grad, route_ids, route_gates, w_gate, w_up, w_down):
    expert_count = lax.axis_size("expert")
    pair_count = lax.axis_size("hid")
    hid_idx = lax.axis_index("hid")
    tok_rows, model_width = tokens.shape
    top_count = route_ids.shape[1]
    capacity = 3 * tok_rows * top_count // (2 * expert_count)
    slot_count = expert_count * capacity
    half_width = model_width // pair_count
    pair_total = tok_rows * top_count
    flat_ids = route_ids.reshape(-1)
    one_hot = (flat_ids[:, None] == jnp.arange(expert_count, dtype=jnp.int32)[None, :]).astype(
        jnp.int32
    )
    earlier = jnp.cumsum(one_hot, axis=0) - one_hot
    slot_index = jnp.sum(earlier * one_hot, axis=1)
    dest_slot = flat_ids * capacity + slot_index
    slot_pair = jnp.zeros((slot_count,), jnp.int32).at[dest_slot].set(
        jnp.arange(pair_total, dtype=jnp.int32)
    )
    slot_token = slot_pair // top_count
    source = jnp.where(hid_idx == 0, tokens, out_grad)
    quad = (expert_count, capacity // 2, 2)
    send = source[slot_token.reshape(quad)]
    recv = lax.all_to_all(send, "expert", split_axis=0, concat_axis=0, tiled=True)
    swap = [(0, 1), (1, 0)]
    other = lax.ppermute(recv, "hid", swap)
    first = hid_idx == 0
    pair_rows = jnp.stack([recv, other])
    rows_x = lax.dynamic_index_in_dim(pair_rows, hid_idx, axis=0, keepdims=False)
    rows_d = lax.dynamic_index_in_dim(pair_rows, 1 - hid_idx, axis=0, keepdims=False)
    gate_mat = w_gate[0]
    up_mat = w_up[0]
    down_mat = w_down[0]
    gate_pre = jnp.einsum("ejqc,cf->ejqf", rows_x, gate_mat, preferred_element_type=jnp.float32)
    up_pre = jnp.einsum("ejqc,cf->ejqf", rows_x, up_mat, preferred_element_type=jnp.float32)
    grad_hidden = jnp.einsum(
        "ejqc,fc->ejqf", rows_d, down_mat, preferred_element_type=jnp.float32
    )
    sigma_gate = jax.nn.sigmoid(gate_pre)
    act_gate = gate_pre * sigma_gate
    score_part = jnp.sum(act_gate * up_pre * grad_hidden, axis=3)
    grad_gate_pre = (
        grad_hidden * up_pre * sigma_gate * (1.0 + gate_pre * (1.0 - sigma_gate))
    ).astype(jnp.bfloat16)
    grad_up_pre = (grad_hidden * act_gate).astype(jnp.bfloat16)
    grad_part = jnp.einsum(
        "ejqf,cf->ejqc", grad_gate_pre, gate_mat, preferred_element_type=jnp.float32
    ) + jnp.einsum("ejqf,cf->ejqc", grad_up_pre, up_mat, preferred_element_type=jnp.float32)
    own_half = lax.dynamic_slice_in_dim(grad_part, hid_idx * half_width, half_width, axis=3)
    give_half = lax.dynamic_slice_in_dim(
        grad_part, (1 - hid_idx) * half_width, half_width, axis=3
    ).astype(jnp.bfloat16)
    got_half = lax.ppermute(give_half, "hid", swap)
    grad_share = (
        own_half.astype(jnp.bfloat16).astype(jnp.float32) + got_half.astype(jnp.float32)
    ).astype(jnp.bfloat16)
    score_full = (score_part + lax.ppermute(score_part, "hid", swap)).astype(jnp.bfloat16)
    score_cols = jnp.zeros(quad + (128,), jnp.bfloat16).at[..., 0].set(score_full)
    back_send = jnp.concatenate([grad_share, score_cols], axis=3)
    back = lax.all_to_all(back_send, "expert", split_axis=0, concat_axis=0, tiled=True)
    route_slot = slot_index.reshape(tok_rows, top_count)
    token_grad = jnp.zeros((tok_rows, half_width), jnp.float32)
    scores = []
    for k in range(top_count):
        row = back[route_ids[:, k], route_slot[:, k] // 2, route_slot[:, k] % 2]
        token_grad = token_grad + row[:, :half_width].astype(jnp.float32) * route_gates[:, k, None]
        scores.append(row[:, half_width])
    token_grad = token_grad.astype(jnp.bfloat16)
    gate_grad = jnp.stack(scores, axis=1)
    return (token_grad, gate_grad)


def solution(mesh):
    return jax.shard_map(
        body,
        mesh=mesh,
        in_specs=(
            P("expert", None),
            P("expert", None),
            P("expert", None),
            P("expert", None),
            P("expert", None, "hid"),
            P("expert", None, "hid"),
            P("expert", "hid", None),
        ),
        out_specs=(P("expert", "hid"), P("expert", None)),
        check_vma=False,
    )
```

```python
import jax
import jax.numpy as jnp
from jax import lax
from jax.sharding import PartitionSpec as P


def body(tokens, out_grad, route_ids, route_gates, w_gate, w_up, w_down):
    expert_count = lax.axis_size("expert")
    pair_count = lax.axis_size("hid")
    hid_idx = lax.axis_index("hid")
    tok_rows, model_width = tokens.shape
    top_count = route_ids.shape[1]
    capacity = 3 * tok_rows * top_count // (2 * expert_count)
    slot_count = expert_count * capacity
    half_width = model_width // pair_count
    pair_total = tok_rows * top_count
    flat_ids = route_ids.reshape(-1)
    one_hot = (flat_ids[:, None] == jnp.arange(expert_count, dtype=jnp.int32)[None, :]).astype(
        jnp.int32
    )
    earlier = jnp.cumsum(one_hot, axis=0) - one_hot
    slot_index = jnp.sum(earlier * one_hot, axis=1)
    dest_slot = flat_ids * capacity + slot_index
    slot_pair = jnp.zeros((slot_count,), jnp.int32).at[dest_slot].set(
        jnp.arange(pair_total, dtype=jnp.int32)
    )
    slot_token = slot_pair // top_count
    source = jnp.where(hid_idx == 0, tokens, out_grad)
    quad = (expert_count, capacity // 2, 2)
    send = source[slot_token.reshape(quad)]
    recv = lax.all_to_all(send, "expert", split_axis=0, concat_axis=0, tiled=True)
    swap = [(0, 1), (1, 0)]
    other = lax.ppermute(recv, "hid", swap)
    first = hid_idx == 0
    rows_x = jnp.where(first, recv, other)
    rows_d = jnp.where(first, other, recv)
    gate_mat = w_gate[0]
    up_mat = w_up[0]
    down_mat = w_down[0]
    gate_pre = jnp.einsum("ejqc,cf->ejqf", rows_x, gate_mat, preferred_element_type=jnp.float32)
    up_pre = jnp.einsum("ejqc,cf->ejqf", rows_x, up_mat, preferred_element_type=jnp.float32)
    grad_hidden = jnp.einsum(
        "ejqc,fc->ejqf", rows_d, down_mat, preferred_element_type=jnp.float32
    )
    sigma_gate = jax.nn.sigmoid(gate_pre)
    act_gate = gate_pre * sigma_gate
    score_part = jnp.sum(act_gate * up_pre * grad_hidden, axis=3)
    grad_gate_pre = (
        grad_hidden * up_pre * sigma_gate * (1.0 + gate_pre * (1.0 - sigma_gate))
    ).astype(jnp.bfloat16)
    grad_up_pre = (grad_hidden * act_gate).astype(jnp.bfloat16)
    grad_part = jnp.einsum(
        "ejqf,cf->ejqc", grad_gate_pre, gate_mat, preferred_element_type=jnp.float32
    ) + jnp.einsum("ejqf,cf->ejqc", grad_up_pre, up_mat, preferred_element_type=jnp.float32)
    own_half = lax.dynamic_slice_in_dim(grad_part, hid_idx * half_width, half_width, axis=3)
    give_half = lax.dynamic_slice_in_dim(
        grad_part, (1 - hid_idx) * half_width, half_width, axis=3
    ).astype(jnp.bfloat16)
    score_block = jnp.zeros(quad + (128,), jnp.float32).at[..., 0].set(score_part)
    give = jnp.concatenate([give_half, score_block.astype(jnp.bfloat16)], axis=3)
    got = lax.ppermute(give, "hid", swap)
    back_send = (
        jnp.concatenate([own_half, score_block], axis=3) + got.astype(jnp.float32)
    ).astype(jnp.bfloat16)
    back = lax.all_to_all(back_send, "expert", split_axis=0, concat_axis=0, tiled=True)
    route_slot = slot_index.reshape(tok_rows, top_count)
    token_grad = jnp.zeros((tok_rows, half_width), jnp.float32)
    scores = []
    for k in range(top_count):
        row = back[route_ids[:, k], route_slot[:, k] // 2, route_slot[:, k] % 2]
        token_grad = token_grad + row[:, :half_width].astype(jnp.float32) * route_gates[:, k, None]
        scores.append(row[:, half_width])
    token_grad = token_grad.astype(jnp.bfloat16)
    gate_grad = jnp.stack(scores, axis=1)
    return (token_grad, gate_grad)


def solution(mesh):
    return jax.shard_map(
        body,
        mesh=mesh,
        in_specs=(
            P("expert", None),
            P("expert", None),
            P("expert", None),
            P("expert", None),
            P("expert", None, "hid"),
            P("expert", None, "hid"),
            P("expert", "hid", None),
        ),
        out_specs=(P("expert", "hid"), P("expert", None)),
        check_vma=False,
    )
```
